256 devices in a mesh: row: 32 (over z, x), col: 8 (over y, core).
Axes of the slice: x: 4, y: 4, z: 8, core: 2. Of those that a mesh axis runs over, the one named last changes fastest.
Arguments:
- kernel: float32 [1, 32, 256, 4, 8, 256], P(None, 'row', None, None, 'col'), as said below
Outputs:
- factor: float32 [1, 32, 256, 4, 8, 256], P(None, 'row', None, None, 'col')
Inputs may be any that keep to these rules, and one draw needn't show every extreme that they name: kernel is a symmetric positive definite matrix.
All inputs are finite; a program needn't handle non-finite values.
Results may differ from the reference program's by a relative error of at most 0.0003.
Values sent between devices are 32-bit elements; how exact they have to be, the bound alone decides.
No kernel may reach another device: no remote copies, remote signals or barrier semaphores. Data moves between devices by JAX's collectives and lax.ppermute only.
A program may use at most 64 MiB of HBM per device.

```python
import math
import jax
import jax.numpy as jnp
from jax import lax

NB = 256
RLOC = 1
PANELS = 2
CLOC = 4
ORDER = 8192


def draw_kernel(key, part):
    embed_width = 768
    raw_vectors = jax.random.normal(jax.random.fold_in(key, 21), (ORDER, embed_width), jnp.float32)
    lengths = jnp.sqrt(jnp.sum(raw_vectors * raw_vectors, axis=1, keepdims=True))
    unit_vectors = raw_vectors / lengths
    inner = jnp.dot(unit_vectors, unit_vectors.T, precision=lax.Precision.HIGHEST)
    inner = 0.5 * (inner + inner.T)
    matrix = jnp.exp(inner - 1.0)
    nugget = jnp.exp(jax.random.uniform(jax.random.fold_in(key, 22), (ORDER,), jnp.float32, math.log(0.01), math.log(0.05)))
    positions = jnp.arange(ORDER, dtype=jnp.int32)
    matrix = matrix.at[positions, positions].add(nugget)
    row_devs = ORDER // (RLOC * NB)
    col_devs = ORDER // (CLOC * NB)
    return matrix.reshape(RLOC, row_devs, NB, CLOC, col_devs, NB)


def setup_inputs(seed: int = 0) -> dict:
    key_of = jax.random.split(jax.random.key(seed), 2)
    kernel = draw_kernel(jax.random.fold_in(key_of[1], 71), 0)
    return {"kernel": kernel}


def reference(kernel):
    matrix = kernel.reshape(ORDER, ORDER)
    for k in range(PANELS):
        start = k * NB
        finish = start + NB
        diag_factor = jnp.linalg.cholesky(matrix[start:finish, start:finish])
        below = matrix[finish:, start:finish]
        below_factor = jax.scipy.linalg.solve_triangular(diag_factor, below.T, lower=True).T
        update_term = jnp.dot(below_factor, below_factor.T, precision=lax.Precision.HIGHEST)
        matrix = matrix.at[finish:, finish:].set(matrix[finish:, finish:] - update_term)
        new_column = jnp.concatenate([jnp.zeros((start, NB), jnp.float32), diag_factor, below_factor], axis=0)
        matrix = matrix.at[:, start:finish].set(new_column)
        matrix = matrix.at[start:finish, finish:].set(jnp.zeros((NB, ORDER - finish), jnp.float32))
    return matrix.reshape(kernel.shape)
```

```python
import jax
import jax.numpy as jnp
from jax import lax
from jax.scipy.linalg import solve_triangular
from jax.sharding import PartitionSpec as P

PANELS = 2
HIGHEST = lax.Precision.HIGHEST


def dot(a, b):
    return jnp.dot(a, b, precision=HIGHEST)


def lead_rows_to_all(tiles):
    block_size, cols_local, _ = tiles.shape
    row_devs = lax.axis_size("row")
    piece = block_size // row_devs
    send = tiles.reshape(row_devs, piece, cols_local, block_size)
    spread = lax.all_to_all(send, "row", 0, 0)[:PANELS]
    send = jnp.broadcast_to(spread[None], (row_devs,) + spread.shape)
    gathered = lax.all_to_all(send, "row", 0, 0)
    return gathered.transpose(1, 0, 2, 3, 4).reshape(PANELS, block_size, cols_local, block_size)


def from_lead_cols(payload):
    col_devs = lax.axis_size("col")
    col_id = lax.axis_index("col")
    have = PANELS
    while have < col_devs:
        pairs = [(i, i + have) for i in range(have) if i + have < col_devs]
        got = lax.ppermute(payload, "col", pairs)
        fresh = (col_id >= have) & (col_id < 2 * have)
        payload = jnp.where(fresh, got, payload)
        have *= 2
    return payload


def shards(kernel):
    _, _, block_size, cols_local, _, _ = kernel.shape
    row_id = lax.axis_index("row")
    col_id = lax.axis_index("col")
    lead = PANELS * block_size
    tiles = kernel.reshape(block_size, cols_local, block_size)

    lead_block = lead_rows_to_all(tiles)

    mine = jnp.stack([tiles[:, 0, :], lead_block[0, :, 0, :], lead_block[1, :, 0, :]])
    other = lax.ppermute(mine, "col", [(0, 1), (1, 0)])
    first, second = jnp.where(col_id == 0, mine, other), jnp.where(col_id == 0, other, mine)
    payload = jnp.stack([first[0], second[0], first[1], first[2], second[2]])
    row_0, row_1, m00, m10, m11 = from_lead_cols(payload)

    lead_matrix = jnp.concatenate(
        [jnp.concatenate([m00, m10.T], axis=1), jnp.concatenate([m10, m11], axis=1)], axis=0
    )
    factor = jnp.linalg.cholesky(lead_matrix)
    inverse = solve_triangular(factor, jnp.eye(lead, dtype=jnp.float32), lower=True)

    right = dot(inverse, lead_block.reshape(lead, cols_local * block_size))
    left = lax.dot_general(
        jnp.concatenate([row_0, row_1], axis=1), inverse, (((1,), (1,)), ((), ())), precision=HIGHEST
    )
    left = jnp.where(
        row_id == 0,
        factor[:block_size],
        jnp.where(row_id == 1, factor[block_size:], left),
    )
    update = dot(left, right).reshape(block_size, cols_local, block_size)
    trailing = jnp.where(row_id >= PANELS, tiles - update, 0.0)
    panel = jnp.where(col_id == 0, left[:, :block_size], left[:, block_size:])
    first_col = jnp.where(col_id < PANELS, panel, trailing[:, 0, :])
    out = trailing.at[:, 0, :].set(first_col)
    return out.reshape(kernel.shape)


def solution(mesh):
    in_specs = (P(None, "row", None, None, "col", None),)
    out_specs = P(None, "row", None, None, "col", None)
    return jax.shard_map(shards, mesh=mesh, in_specs=in_specs, out_specs=out_specs, check_vma=False)
```

```python
import jax
import jax.numpy as jnp
from jax import lax
from jax.scipy.linalg import solve_triangular
from jax.sharding import PartitionSpec as P

PANELS = 2
HIGHEST = lax.Precision.HIGHEST


def dot(a, b):
    return jnp.dot(a, b, precision=HIGHEST)


def lead_rows_to_all(tiles):
    block_size, cols_local, _ = tiles.shape
    row_devs = lax.axis_size("row")
    piece = block_size // row_devs
    send = tiles.reshape(row_devs, piece, cols_local, block_size)
    spread = lax.all_to_all(send, "row", 0, 0)[:PANELS]
    send = jnp.broadcast_to(spread[None], (row_devs,) + spread.shape)
    gathered = lax.all_to_all(send, "row", 0, 0)
    return gathered.transpose(1, 0, 2, 3, 4).reshape(PANELS, block_size, cols_local, block_size)


def from_lead_cols(payload):
    col_devs = lax.axis_size("col")
    col_id = lax.axis_index("col")
    have = PANELS
    while have < col_devs:
        pairs = [(i, i + have) for i in range(have) if i + have < col_devs]
        got = lax.ppermute(payload, "col", pairs)
        fresh = (col_id >= have) & (col_id < 2 * have)
        payload = jnp.where(fresh, got, payload)
        have *= 2
    return payload


def blocked_factor(matrix, step):
    count = matrix.shape[0] // step
    blocks = [[matrix[i * step:(i + 1) * step, j * step:(j + 1) * step] for j in range(count)] for i in range(count)]
    eye = jnp.eye(step, dtype=jnp.float32)
    low = [[None] * count for _ in range(count)]
    inv_diag = []
    for k in range(count):
        diag = jnp.linalg.cholesky(blocks[k][k])
        inv = solve_triangular(diag, eye, lower=True)
        low[k][k] = diag
        inv_diag.append(inv)
        if k + 1 < count:
            below = jnp.concatenate([blocks[i][k] for i in range(k + 1, count)], axis=0)
            below = lax.dot_general(below, inv, (((1,), (1,)), ((), ())), precision=HIGHEST)
            for i in range(k + 1, count):
                low[i][k] = below[(i - k - 1) * step:(i - k) * step]
            shrink = lax.dot_general(below, below, (((1,), (1,)), ((), ())), precision=HIGHEST)
            for i in range(k + 1, count):
                for j in range(k + 1, i + 1):
                    blocks[i][j] = blocks[i][j] - shrink[(i - k - 1) * step:(i - k) * step, (j - k - 1) * step:(j - k) * step]
    inverse = [[None] * count for _ in range(count)]
    for j in range(count):
        inverse[j][j] = inv_diag[j]
        for i in range(j + 1, count):
            acc = dot(low[i][j], inverse[j][j])
            for k in range(j + 1, i):
                acc = acc + dot(low[i][k], inverse[k][j])
            inverse[i][j] = -dot(inv_diag[i], acc)
    zero = jnp.zeros((step, step), jnp.float32)
    factor = jnp.block([[low[i][j] if j <= i else zero for j in range(count)] for i in range(count)])
    inverse = jnp.block([[inverse[i][j] if j <= i else zero for j in range(count)] for i in range(count)])
    return factor, inverse


def shards(kernel):
    _, _, block_size, cols_local, _, _ = kernel.shape
    row_id = lax.axis_index("row")
    col_id = lax.axis_index("col")
    lead = PANELS * block_size
    tiles = kernel.reshape(block_size, cols_local, block_size)

    own = tiles[:, 0, :]
    other = lax.ppermute(own, "col", [(0, 1), (1, 0)])
    row_panel = jnp.where(col_id == 0, jnp.stack([own, other]), jnp.stack([other, own]))
    row_0, row_1 = from_lead_cols(row_panel)

    lead_block = lead_rows_to_all(tiles)

    mine = jnp.stack([lead_block[0, :, 0, :], lead_block[1, :, 0, :]])
    other = lax.ppermute(mine, "col", [(0, 1), (1, 0)])
    first, second = jnp.where(col_id == 0, mine, other), jnp.where(col_id == 0, other, mine)
    m00, m10, m11 = from_lead_cols(jnp.stack([first[0], first[1], second[1]]))

    lead_matrix = jnp.concatenate(
        [jnp.concatenate([m00, m10.T], axis=1), jnp.concatenate([m10, m11], axis=1)], axis=0
    )
    factor, inverse = blocked_factor(lead_matrix, 128)

    right = dot(inverse, lead_block.reshape(lead, cols_local * block_size))
    left = lax.dot_general(
        jnp.concatenate([row_0, row_1], axis=1), inverse, (((1,), (1,)), ((), ())), precision=HIGHEST
    )
    left = jnp.where(
        row_id == 0,
        factor[:block_size],
        jnp.where(row_id == 1, factor[block_size:], left),
    )
    update = dot(left, right).reshape(block_size, cols_local, block_size)
    trailing = jnp.where(row_id >= PANELS, tiles - update, 0.0)
    panel = jnp.where(col_id == 0, left[:, :block_size], left[:, block_size:])
    first_col = jnp.where(col_id < PANELS, panel, trailing[:, 0, :])
    out = trailing.at[:, 0, :].set(first_col)
    return out.reshape(kernel.shape)


def solution(mesh):
    in_specs = (P(None, "row", None, None, "col", None),)
    out_specs = P(None, "row", None, None, "col", None)
    return jax.shard_map(shards, mesh=mesh, in_specs=in_specs, out_specs=out_specs, check_vma=False)
```

```python
import jax
import jax.numpy as jnp
from jax import lax
from jax.scipy.linalg import solve_triangular
from jax.sharding import PartitionSpec as P

PANELS = 2
HIGHEST = lax.Precision.HIGHEST


def dot(a, b):
    return jnp.dot(a, b, precision=HIGHEST)


def col_rounds(have=PANELS):
    col_devs = lax.axis_size("col")
    rounds = []
    while have < col_devs:
        rounds.append((have, [(i, i + have) for i in range(have) if i + have < col_devs]))
        have *= 2
    return rounds


def tree_round(payload, have, pairs):
    col_id = lax.axis_index("col")
    got = lax.ppermute(payload, "col", pairs)
    return jnp.where((col_id >= have) & (col_id < 2 * have), got, payload)


def from_lead_cols(payload, have=PANELS):
    for have, pairs in col_rounds(have):
        payload = tree_round(payload, have, pairs)
    return payload


def swap_lead_cols(mine):
    col_id = lax.axis_index("col")
    other = lax.ppermute(mine, "col", [(0, 1), (1, 0)])
    return jnp.where(col_id == 0, mine, other), jnp.where(col_id == 0, other, mine)


def blocked_factor(matrix, step):
    count = matrix.shape[0] // step
    blocks = [[matrix[i * step:(i + 1) * step, j * step:(j + 1) * step] for j in range(count)] for i in range(count)]
    eye = jnp.eye(step, dtype=jnp.float32)
    low = [[None] * count for _ in range(count)]
    inv_diag = []
    for k in range(count):
        diag = jnp.linalg.cholesky(blocks[k][k])
        inv = solve_triangular(diag, eye, lower=True)
        low[k][k] = diag
        inv_diag.append(inv)
        if k + 1 < count:
            below = jnp.concatenate([blocks[i][k] for i in range(k + 1, count)], axis=0)
            below = lax.dot_general(below, inv, (((1,), (1,)), ((), ())), precision=HIGHEST)
            for i in range(k + 1, count):
                low[i][k] = below[(i - k - 1) * step:(i - k) * step]
            shrink = lax.dot_general(below, below, (((1,), (1,)), ((), ())), precision=HIGHEST)
            for i in range(k + 1, count):
                for j in range(k + 1, i + 1):
                    blocks[i][j] = blocks[i][j] - shrink[(i - k - 1) * step:(i - k) * step, (j - k - 1) * step:(j - k) * step]
    inverse = [[None] * count for _ in range(count)]
    for j in range(count):
        inverse[j][j] = inv_diag[j]
        for i in range(j + 1, count):
            acc = dot(low[i][j], inverse[j][j])
            for k in range(j + 1, i):
                acc = acc + dot(low[i][k], inverse[k][j])
            inverse[i][j] = -dot(inv_diag[i], acc)
    zero = jnp.zeros((step, step), jnp.float32)
    factor = jnp.block([[low[i][j] if j <= i else zero for j in range(count)] for i in range(count)])
    inverse = jnp.block([[inverse[i][j] if j <= i else zero for j in range(count)] for i in range(count)])
    return factor, inverse


def shards(kernel):
    _, _, block_size, cols_local, _, _ = kernel.shape
    row_devs = lax.axis_size("row")
    row_id = lax.axis_index("row")
    col_id = lax.axis_index("col")
    lead = PANELS * block_size
    piece = block_size // row_devs
    tiles = kernel.reshape(block_size, cols_local, block_size)

    first, second = swap_lead_cols(tiles[:, 0, :])
    row_panel = jnp.stack([first, second])
    rounds = col_rounds()
    tiles_now, row_panel = lax.optimization_barrier((tiles, row_panel))

    send = tiles_now.reshape(row_devs, piece, cols_local, block_size)
    spread = lax.all_to_all(send, "row", 0, 0)[:PANELS]
    if rounds:
        row_panel = tree_round(row_panel, *rounds[0])
        spread, row_panel = lax.optimization_barrier((spread, row_panel))
    send = jnp.broadcast_to(spread[None], (row_devs,) + spread.shape)
    gathered = lax.all_to_all(send, "row", 0, 0)
    for have, pairs in rounds[1:]:
        row_panel = tree_round(row_panel, have, pairs)
    gathered, row_panel = lax.optimization_barrier((gathered, row_panel))
    lead_block = gathered.transpose(1, 0, 2, 3, 4).reshape(PANELS, block_size, cols_local, block_size)
    row_0, row_1 = row_panel

    m00 = from_lead_cols(lead_block[0, :, 0, :], 1)
    first, second = swap_lead_cols(lead_block[1, :, 0, :])
    m10, m11 = from_lead_cols(jnp.stack([first, second]))

    d0, g0 = blocked_factor(m00, 128)
    l10 = lax.dot_general(m10, g0, (((1,), (1,)), ((), ())), precision=HIGHEST)
    schur = m11 - lax.dot_general(l10, l10, (((1,), (1,)), ((), ())), precision=HIGHEST)
    d1, g1 = blocked_factor(schur, 128)
    g10 = -dot(g1, dot(l10, g0))
    zero = jnp.zeros_like(d0)
    factor = jnp.block([[d0, zero], [l10, d1]])
    inverse = jnp.block([[g0, zero], [g10, g1]])

    right = dot(inverse, lead_block.reshape(lead, cols_local * block_size))
    left = lax.dot_general(
        jnp.concatenate([row_0, row_1], axis=1), inverse, (((1,), (1,)), ((), ())), precision=HIGHEST
    )
    left = jnp.where(
        row_id == 0,
        factor[:block_size],
        jnp.where(row_id == 1, factor[block_size:], left),
    )
    update = dot(left, right).reshape(block_size, cols_local, block_size)
    trailing = jnp.where(row_id >= PANELS, tiles - update, 0.0)
    panel = jnp.where(col_id == 0, left[:, :block_size], left[:, block_size:])
    first_col = jnp.where(col_id < PANELS, panel, trailing[:, 0, :])
    out = trailing.at[:, 0, :].set(first_col)
    return out.reshape(kernel.shape)


def solution(mesh):
    in_specs = (P(None, "row", None, None, "col", None),)
    out_specs = P(None, "row", None, None, "col", None)
    return jax.shard_map(shards, mesh=mesh, in_specs=in_specs, out_specs=out_specs, check_vma=False)
```

```python
import jax
import jax.numpy as jnp
from jax import lax
from jax.scipy.linalg import solve_triangular
from jax.sharding import PartitionSpec as P

PANELS = 2
HIGHEST = lax.Precision.HIGHEST


def dot(a, b):
    return jnp.dot(a, b, precision=HIGHEST)


def col_rounds(have=PANELS):
    col_devs = lax.axis_size("col")
    rounds = []
    while have < col_devs:
        rounds.append((have, [(i, i + have) for i in range(have) if i + have < col_devs]))
        have *= 2
    return rounds


def tree_round(payload, have, pairs):
    col_id = lax.axis_index("col")
    got = lax.ppermute(payload, "col", pairs)
    return jnp.where((col_id >= have) & (col_id < 2 * have), got, payload)


def from_lead_cols(payload, have=PANELS):
    for have, pairs in col_rounds(have):
        payload = tree_round(payload, have, pairs)
    return payload


def swap_lead_cols(mine):
    col_id = lax.axis_index("col")
    other = lax.ppermute(mine, "col", [(0, 1), (1, 0)])
    return jnp.where(col_id == 0, mine, other), jnp.where(col_id == 0, other, mine)


def blocked_factor(matrix, step):
    count = matrix.shape[0] // step
    blocks = [[matrix[i * step:(i + 1) * step, j * step:(j + 1) * step] for j in range(count)] for i in range(count)]
    eye = jnp.eye(step, dtype=jnp.float32)
    low = [[None] * count for _ in range(count)]
    inv_diag = []
    for k in range(count):
        diag = jnp.linalg.cholesky(blocks[k][k])
        inv = solve_triangular(diag, eye, lower=True)
        low[k][k] = diag
        inv_diag.append(inv)
        if k + 1 < count:
            below = jnp.concatenate([blocks[i][k] for i in range(k + 1, count)], axis=0)
            below = lax.dot_general(below, inv, (((1,), (1,)), ((), ())), precision=HIGHEST)
            for i in range(k + 1, count):
                low[i][k] = below[(i - k - 1) * step:(i - k) * step]
            shrink = lax.dot_general(below, below, (((1,), (1,)), ((), ())), precision=HIGHEST)
            for i in range(k + 1, count):
                for j in range(k + 1, i + 1):
                    blocks[i][j] = blocks[i][j] - shrink[(i - k - 1) * step:(i - k) * step, (j - k - 1) * step:(j - k) * step]
    inverse = [[None] * count for _ in range(count)]
    for j in range(count):
        inverse[j][j] = inv_diag[j]
        for i in range(j + 1, count):
            acc = dot(low[i][j], inverse[j][j])
            for k in range(j + 1, i):
                acc = acc + dot(low[i][k], inverse[k][j])
            inverse[i][j] = -dot(inv_diag[i], acc)
    zero = jnp.zeros((step, step), jnp.float32)
    factor = jnp.block([[low[i][j] if j <= i else zero for j in range(count)] for i in range(count)])
    inverse = jnp.block([[inverse[i][j] if j <= i else zero for j in range(count)] for i in range(count)])
    return factor, inverse


def row_broadcast(blocks, source=0):
    row_devs = lax.axis_size("row")
    shape = blocks.shape
    send = blocks.reshape(row_devs, -1)
    piece = lax.all_to_all(send, "row", 0, 0)[source]
    send = jnp.broadcast_to(piece[None], (row_devs,) + piece.shape)
    return lax.all_to_all(send, "row", 0, 0).reshape(shape)


def shards(kernel):
    _, _, block_size, cols_local, _, _ = kernel.shape
    row_devs = lax.axis_size("row")
    row_id = lax.axis_index("row")
    col_id = lax.axis_index("col")
    lead = PANELS * block_size
    piece = block_size // row_devs
    tiles = kernel.reshape(block_size, cols_local, block_size)

    own = tiles[:, 0, :]
    swapped = lax.ppermute(own, "row", [(0, 1), (1, 0)])
    first, second = swap_lead_cols(jnp.stack([own, swapped]))
    held = from_lead_cols(jnp.concatenate([first, second]))

    send = tiles.reshape(row_devs, piece, cols_local, block_size)
    spread = lax.all_to_all(send, "row", 0, 0)[:PANELS]
    spread, held = lax.optimization_barrier((spread, held))
    row_0, row_1 = held[0], held[2]
    lead_blocks = jnp.where(row_id == 0, held[jnp.array([0, 1, 3])], held[jnp.array([1, 0, 2])])

    m00, m10, m11 = row_broadcast(lead_blocks)
    spread, m00 = lax.optimization_barrier((spread, m00))

    send = jnp.broadcast_to(spread[None], (row_devs,) + spread.shape)
    gathered = lax.all_to_all(send, "row", 0, 0)
    lead_block = gathered.transpose(1, 0, 2, 3, 4).reshape(PANELS, block_size, cols_local, block_size)

    d0, g0 = blocked_factor(m00, 128)
    l10 = lax.dot_general(m10, g0, (((1,), (1,)), ((), ())), precision=HIGHEST)
    schur = m11 - lax.dot_general(l10, l10, (((1,), (1,)), ((), ())), precision=HIGHEST)
    d1, g1 = blocked_factor(schur, 128)
    g10 = -dot(g1, dot(l10, g0))
    zero = jnp.zeros_like(d0)
    factor = jnp.block([[d0, zero], [l10, d1]])
    inverse = jnp.block([[g0, zero], [g10, g1]])

    right = dot(inverse, lead_block.reshape(lead, cols_local * block_size))
    left = lax.dot_general(
        jnp.concatenate([row_0, row_1], axis=1), inverse, (((1,), (1,)), ((), ())), precision=HIGHEST
    )
    left = jnp.where(
        row_id == 0,
        factor[:block_size],
        jnp.where(row_id == 1, factor[block_size:], left),
    )
    update = dot(left, right).reshape(block_size, cols_local, block_size)
    trailing = jnp.where(row_id >= PANELS, tiles - update, 0.0)
    panel = jnp.where(col_id == 0, left[:, :block_size], left[:, block_size:])
    first_col = jnp.where(col_id < PANELS, panel, trailing[:, 0, :])
    out = trailing.at[:, 0, :].set(first_col)
    return out.reshape(kernel.shape)


def solution(mesh):
    in_specs = (P(None, "row", None, None, "col", None),)
    out_specs = P(None, "row", None, None, "col", None)
    return jax.shard_map(shards, mesh=mesh, in_specs=in_specs, out_specs=out_specs, check_vma=False)
```

```python
import jax
import jax.numpy as jnp
from jax import lax
from jax.scipy.linalg import solve_triangular
from jax.sharding import PartitionSpec as P

PANELS = 2
HIGHEST = lax.Precision.HIGHEST


def dot(a, b):
    return jnp.dot(a, b, precision=HIGHEST)


def col_rounds(have=PANELS):
    col_devs = lax.axis_size("col")
    rounds = []
    while have < col_devs:
        rounds.append((have, [(i, i + have) for i in range(have) if i + have < col_devs]))
        have *= 2
    return rounds


def tree_round(payload, have, pairs):
    col_id = lax.axis_index("col")
    got = lax.ppermute(payload, "col", pairs)
    return jnp.where((col_id >= have) & (col_id < 2 * have), got, payload)


def from_lead_cols(payload, have=PANELS):
    for have, pairs in col_rounds(have):
        payload = tree_round(payload, have, pairs)
    return payload


def swap_lead_cols(mine):
    col_id = lax.axis_index("col")
    other = lax.ppermute(mine, "col", [(0, 1), (1, 0)])
    return jnp.where(col_id == 0, mine, other), jnp.where(col_id == 0, other, mine)


def blocked_factor(matrix, step):
    count = matrix.shape[0] // step
    blocks = [[matrix[i * step:(i + 1) * step, j * step:(j + 1) * step] for j in range(count)] for i in range(count)]
    eye = jnp.eye(step, dtype=jnp.float32)
    low = [[None] * count for _ in range(count)]
    inv_diag = []
    for k in range(count):
        diag = jnp.linalg.cholesky(blocks[k][k])
        inv = solve_triangular(diag, eye, lower=True)
        low[k][k] = diag
        inv_diag.append(inv)
        if k + 1 < count:
            below = jnp.concatenate([blocks[i][k] for i in range(k + 1, count)], axis=0)
            below = lax.dot_general(below, inv, (((1,), (1,)), ((), ())), precision=HIGHEST)
            for i in range(k + 1, count):
                low[i][k] = below[(i - k - 1) * step:(i - k) * step]
            shrink = lax.dot_general(below, below, (((1,), (1,)), ((), ())), precision=HIGHEST)
            for i in range(k + 1, count):
                for j in range(k + 1, i + 1):
                    blocks[i][j] = blocks[i][j] - shrink[(i - k - 1) * step:(i - k) * step, (j - k - 1) * step:(j - k) * step]
    inverse = [[None] * count for _ in range(count)]
    for j in range(count):
        inverse[j][j] = inv_diag[j]
        for i in range(j + 1, count):
            acc = dot(low[i][j], inverse[j][j])
            for k in range(j + 1, i):
                acc = acc + dot(low[i][k], inverse[k][j])
            inverse[i][j] = -dot(inv_diag[i], acc)
    zero = jnp.zeros((step, step), jnp.float32)
    factor = jnp.block([[low[i][j] if j <= i else zero for j in range(count)] for i in range(count)])
    inverse = jnp.block([[inverse[i][j] if j <= i else zero for j in range(count)] for i in range(count)])
    return factor, inverse


def row_broadcast(blocks, source=0):
    row_devs = lax.axis_size("row")
    shape = blocks.shape
    send = blocks.reshape(row_devs, -1)
    piece = lax.all_to_all(send, "row", 0, 0)[source]
    send = jnp.broadcast_to(piece[None], (row_devs,) + piece.shape)
    return lax.all_to_all(send, "row", 0, 0).reshape(shape)


def gather_rows(spread):
    row_devs = lax.axis_size("row")
    send = jnp.broadcast_to(spread[None], (row_devs,) + spread.shape)
    gathered = lax.all_to_all(send, "row", 0, 0)
    return gathered.swapaxes(0, 1)


def shards(kernel):
    _, _, block_size, cols_local, _, _ = kernel.shape
    row_devs = lax.axis_size("row")
    row_id = lax.axis_index("row")
    col_id = lax.axis_index("col")
    lead = PANELS * block_size
    piece = block_size // row_devs
    tiles = kernel.reshape(block_size, cols_local, block_size)

    send = tiles.reshape(row_devs, piece, cols_local, block_size)
    spread = lax.all_to_all(send, "row", 0, 0)[:PANELS]

    lead_0 = gather_rows(spread[:, :, 0, :]).reshape(PANELS, block_size, block_size)
    first, second = swap_lead_cols(lead_0)
    m00, m10, m11 = from_lead_cols(jnp.stack([first[0], first[1], second[1]]))
    spread, own, m00 = lax.optimization_barrier((spread, tiles[:, 0, :], m00))

    first, second = swap_lead_cols(own)
    row_0, row_1 = from_lead_cols(jnp.stack([first, second]))

    rest = gather_rows(spread[:, :, 1:, :]).reshape(PANELS, block_size, cols_local - 1, block_size)
    lead_block = jnp.concatenate([lead_0[:, :, None, :], rest], axis=2)

    d0, g0 = blocked_factor(m00, 128)
    l10 = lax.dot_general(m10, g0, (((1,), (1,)), ((), ())), precision=HIGHEST)
    schur = m11 - lax.dot_general(l10, l10, (((1,), (1,)), ((), ())), precision=HIGHEST)
    schur, row_0, row_1 = lax.optimization_barrier((schur, row_0, row_1))
    d1, g1 = blocked_factor(schur, 128)
    g10 = -dot(g1, dot(l10, g0))
    zero = jnp.zeros_like(d0)
    factor = jnp.block([[d0, zero], [l10, d1]])
    inverse = jnp.block([[g0, zero], [g10, g1]])

    right = dot(inverse, lead_block.reshape(lead, cols_local * block_size))
    left = lax.dot_general(
        jnp.concatenate([row_0, row_1], axis=1), inverse, (((1,), (1,)), ((), ())), precision=HIGHEST
    )
    left = jnp.where(
        row_id == 0,
        factor[:block_size],
        jnp.where(row_id == 1, factor[block_size:], left),
    )
    update = dot(left, right).reshape(block_size, cols_local, block_size)
    trailing = jnp.where(row_id >= PANELS, tiles - update, 0.0)
    panel = jnp.where(col_id == 0, left[:, :block_size], left[:, block_size:])
    first_col = jnp.where(col_id < PANELS, panel, trailing[:, 0, :])
    out = trailing.at[:, 0, :].set(first_col)
    return out.reshape(kernel.shape)


def solution(mesh):
    in_specs = (P(None, "row", None, None, "col", None),)
    out_specs = P(None, "row", None, None, "col", None)
    return jax.shard_map(shards, mesh=mesh, in_specs=in_specs, out_specs=out_specs, check_vma=False)
```

```python
import jax
import jax.numpy as jnp
from jax import lax
from jax.scipy.linalg import solve_triangular
from jax.sharding import PartitionSpec as P

PANELS = 2
HIGHEST = lax.Precision.HIGHEST


def dot(a, b):
    return jnp.dot(a, b, precision=HIGHEST)


def col_rounds(have=PANELS):
    col_devs = lax.axis_size("col")
    rounds = []
    while have < col_devs:
        rounds.append((have, [(i, i + have) for i in range(have) if i + have < col_devs]))
        have *= 2
    return rounds


def tree_round(payload, have, pairs):
    col_id = lax.axis_index("col")
    got = lax.ppermute(payload, "col", pairs)
    return jnp.where((col_id >= have) & (col_id < 2 * have), got, payload)


def from_lead_cols(payload, have=PANELS):
    for have, pairs in col_rounds(have):
        payload = tree_round(payload, have, pairs)
    return payload


def swap_lead_cols(mine):
    col_id = lax.axis_index("col")
    other = lax.ppermute(mine, "col", [(0, 1), (1, 0)])
    return jnp.where(col_id == 0, mine, other), jnp.where(col_id == 0, other, mine)


def blocked_factor(matrix, step):
    count = matrix.shape[0] // step
    blocks = [[matrix[i * step:(i + 1) * step, j * step:(j + 1) * step] for j in range(count)] for i in range(count)]
    eye = jnp.eye(step, dtype=jnp.float32)
    low = [[None] * count for _ in range(count)]
    inv_diag = []
    for k in range(count):
        diag = jnp.linalg.cholesky(blocks[k][k])
        inv = solve_triangular(diag, eye, lower=True)
        low[k][k] = diag
        inv_diag.append(inv)
        if k + 1 < count:
            below = jnp.concatenate([blocks[i][k] for i in range(k + 1, count)], axis=0)
            below = lax.dot_general(below, inv, (((1,), (1,)), ((), ())), precision=HIGHEST)
            for i in range(k + 1, count):
                low[i][k] = below[(i - k - 1) * step:(i - k) * step]
            shrink = lax.dot_general(below, below, (((1,), (1,)), ((), ())), precision=HIGHEST)
            for i in range(k + 1, count):
                for j in range(k + 1, i + 1):
                    blocks[i][j] = blocks[i][j] - shrink[(i - k - 1) * step:(i - k) * step, (j - k - 1) * step:(j - k) * step]
    inverse = [[None] * count for _ in range(count)]
    for j in range(count):
        inverse[j][j] = inv_diag[j]
        for i in range(j + 1, count):
            acc = dot(low[i][j], inverse[j][j])
            for k in range(j + 1, i):
                acc = acc + dot(low[i][k], inverse[k][j])
            inverse[i][j] = -dot(inv_diag[i], acc)
    zero = jnp.zeros((step, step), jnp.float32)
    factor = jnp.block([[low[i][j] if j <= i else zero for j in range(count)] for i in range(count)])
    inverse = jnp.block([[inverse[i][j] if j <= i else zero for j in range(count)] for i in range(count)])
    return factor, inverse


def row_broadcast(blocks, source=0):
    row_devs = lax.axis_size("row")
    shape = blocks.shape
    send = blocks.reshape(row_devs, -1)
    piece = lax.all_to_all(send, "row", 0, 0)[source]
    send = jnp.broadcast_to(piece[None], (row_devs,) + piece.shape)
    return lax.all_to_all(send, "row", 0, 0).reshape(shape)


def lead_rows_from(blocks):
    row_devs = lax.axis_size("row")
    send = blocks.reshape(row_devs, -1)
    piece = lax.all_to_all(send, "row", 0, 0)[:PANELS]
    send = jnp.broadcast_to(piece[None], (row_devs,) + piece.shape)
    gathered = lax.all_to_all(send, "row", 0, 0)
    return gathered.swapaxes(0, 1).reshape((PANELS,) + blocks.shape)


def shards(kernel):
    _, _, block_size, cols_local, _, _ = kernel.shape
    row_devs = lax.axis_size("row")
    row_id = lax.axis_index("row")
    col_id = lax.axis_index("col")
    lead = PANELS * block_size
    piece = block_size // row_devs
    tiles = kernel.reshape(block_size, cols_local, block_size)

    first, second = swap_lead_cols(tiles[:, 0, :])
    held = from_lead_cols(jnp.stack([first, second]))

    send = tiles.reshape(row_devs, piece, cols_local, block_size)
    spread = lax.all_to_all(send, "row", 0, 0)[:PANELS]
    spread, held = lax.optimization_barrier((spread, held))
    row_0, row_1 = held[0], held[1]

    lead_rows = lead_rows_from(held)
    m00, m10, m11 = lead_rows[0, 0], lead_rows[1, 0], lead_rows[1, 1]
    spread, m00 = lax.optimization_barrier((spread, m00))

    send = jnp.broadcast_to(spread[None], (row_devs,) + spread.shape)
    gathered = lax.all_to_all(send, "row", 0, 0)
    lead_block = gathered.transpose(1, 0, 2, 3, 4).reshape(PANELS, block_size, cols_local, block_size)

    d0, g0 = blocked_factor(m00, 128)
    l10 = lax.dot_general(m10, g0, (((1,), (1,)), ((), ())), precision=HIGHEST)
    schur = m11 - lax.dot_general(l10, l10, (((1,), (1,)), ((), ())), precision=HIGHEST)
    d1, g1 = blocked_factor(schur, 128)
    g10 = -dot(g1, dot(l10, g0))
    zero = jnp.zeros_like(d0)
    factor = jnp.block([[d0, zero], [l10, d1]])
    inverse = jnp.block([[g0, zero], [g10, g1]])

    right = dot(inverse, lead_block.reshape(lead, cols_local * block_size))
    left = lax.dot_general(
        jnp.concatenate([row_0, row_1], axis=1), inverse, (((1,), (1,)), ((), ())), precision=HIGHEST
    )
    left = jnp.where(
        row_id == 0,
        factor[:block_size],
        jnp.where(row_id == 1, factor[block_size:], left),
    )
    update = dot(left, right).reshape(block_size, cols_local, block_size)
    trailing = jnp.where(row_id >= PANELS, tiles - update, 0.0)
    panel = jnp.where(col_id == 0, left[:, :block_size], left[:, block_size:])
    first_col = jnp.where(col_id < PANELS, panel, trailing[:, 0, :])
    out = trailing.at[:, 0, :].set(first_col)
    return out.reshape(kernel.shape)


def solution(mesh):
    in_specs = (P(None, "row", None, None, "col", None),)
    out_specs = P(None, "row", None, None, "col", None)
    return jax.shard_map(shards, mesh=mesh, in_specs=in_specs, out_specs=out_specs, check_vma=False)
```

```python
import jax
import jax.numpy as jnp
from jax import lax
from jax.scipy.linalg import solve_triangular
from jax.sharding import PartitionSpec as P

PANELS = 2
HIGHEST = lax.Precision.HIGHEST


def dot(a, b):
    return jnp.dot(a, b, precision=HIGHEST)


def col_rounds(have=PANELS):
    col_devs = lax.axis_size("col")
    rounds = []
    while have < col_devs:
        rounds.append((have, [(i, i + have) for i in range(have) if i + have < col_devs]))
        have *= 2
    return rounds


def tree_round(payload, have, pairs):
    col_id = lax.axis_index("col")
    got = lax.ppermute(payload, "col", pairs)
    return jnp.where((col_id >= have) & (col_id < 2 * have), got, payload)


def from_lead_cols(payload, have=PANELS):
    for have, pairs in col_rounds(have):
        payload = tree_round(payload, have, pairs)
    return payload


def swap_lead_cols(mine):
    col_id = lax.axis_index("col")
    other = lax.ppermute(mine, "col", [(0, 1), (1, 0)])
    return jnp.where(col_id == 0, mine, other), jnp.where(col_id == 0, other, mine)


def blocked_factor(matrix, step):
    count = matrix.shape[0] // step
    blocks = [[matrix[i * step:(i + 1) * step, j * step:(j + 1) * step] for j in range(count)] for i in range(count)]
    eye = jnp.eye(step, dtype=jnp.float32)
    low = [[None] * count for _ in range(count)]
    inv_diag = []
    for k in range(count):
        diag = jnp.linalg.cholesky(blocks[k][k])
        inv = solve_triangular(diag, eye, lower=True)
        low[k][k] = diag
        inv_diag.append(inv)
        if k + 1 < count:
            below = jnp.concatenate([blocks[i][k] for i in range(k + 1, count)], axis=0)
            below = lax.dot_general(below, inv, (((1,), (1,)), ((), ())), precision=HIGHEST)
            for i in range(k + 1, count):
                low[i][k] = below[(i - k - 1) * step:(i - k) * step]
            shrink = lax.dot_general(below, below, (((1,), (1,)), ((), ())), precision=HIGHEST)
            for i in range(k + 1, count):
                for j in range(k + 1, i + 1):
                    blocks[i][j] = blocks[i][j] - shrink[(i - k - 1) * step:(i - k) * step, (j - k - 1) * step:(j - k) * step]
    inverse = [[None] * count for _ in range(count)]
    for j in range(count):
        inverse[j][j] = inv_diag[j]
        for i in range(j + 1, count):
            acc = dot(low[i][j], inverse[j][j])
            for k in range(j + 1, i):
                acc = acc + dot(low[i][k], inverse[k][j])
            inverse[i][j] = -dot(inv_diag[i], acc)
    zero = jnp.zeros((step, step), jnp.float32)
    factor = jnp.block([[low[i][j] if j <= i else zero for j in range(count)] for i in range(count)])
    inverse = jnp.block([[inverse[i][j] if j <= i else zero for j in range(count)] for i in range(count)])
    return factor, inverse


def row_broadcast(blocks, source=0):
    row_devs = lax.axis_size("row")
    shape = blocks.shape
    send = blocks.reshape(row_devs, -1)
    piece = lax.all_to_all(send, "row", 0, 0)[source]
    send = jnp.broadcast_to(piece[None], (row_devs,) + piece.shape)
    return lax.all_to_all(send, "row", 0, 0).reshape(shape)


def lead_rows_from(blocks):
    row_devs = lax.axis_size("row")
    send = blocks.reshape(row_devs, -1)
    piece = lax.all_to_all(send, "row", 0, 0)[:PANELS]
    send = jnp.broadcast_to(piece[None], (row_devs,) + piece.shape)
    gathered = lax.all_to_all(send, "row", 0, 0)
    return gathered.swapaxes(0, 1).reshape((PANELS,) + blocks.shape)


def shards(kernel):
    _, _, block_size, cols_local, _, _ = kernel.shape
    row_devs = lax.axis_size("row")
    row_id = lax.axis_index("row")
    col_id = lax.axis_index("col")
    lead = PANELS * block_size
    piece = block_size // row_devs
    tiles = kernel.reshape(block_size, cols_local, block_size)

    first, second = swap_lead_cols(tiles[:, 0, :])
    held = from_lead_cols(jnp.stack([first, second]))

    send = tiles.reshape(row_devs, piece, cols_local, block_size)
    spread = lax.all_to_all(send, "row", 0, 0)[:PANELS]
    spread, held = lax.optimization_barrier((spread, held))
    row_0, row_1 = held[0], held[1]

    half = block_size // 2
    size = block_size * block_size
    from_row_0 = jnp.concatenate([held[0].ravel(), held[1][:, :half].ravel()])
    from_row_1 = jnp.concatenate([held[1].ravel(), held[0][half:, :].ravel()])
    lead_rows = lead_rows_from(jnp.where(row_id == 0, from_row_0, from_row_1))
    m00 = lead_rows[0, :size].reshape(block_size, block_size)
    m11 = lead_rows[1, :size].reshape(block_size, block_size)
    m10 = jnp.concatenate(
        [lead_rows[0, size:].reshape(block_size, half).T, lead_rows[1, size:].reshape(half, block_size)]
    )
    spread, m00 = lax.optimization_barrier((spread, m00))

    send = jnp.broadcast_to(spread[None], (row_devs,) + spread.shape)
    gathered = lax.all_to_all(send, "row", 0, 0)
    lead_block = gathered.transpose(1, 0, 2, 3, 4).reshape(PANELS, block_size, cols_local, block_size)

    d0, g0 = blocked_factor(m00, 128)
    l10 = lax.dot_general(m10, g0, (((1,), (1,)), ((), ())), precision=HIGHEST)
    schur = m11 - lax.dot_general(l10, l10, (((1,), (1,)), ((), ())), precision=HIGHEST)
    d1, g1 = blocked_factor(schur, 128)
    g10 = -dot(g1, dot(l10, g0))
    zero = jnp.zeros_like(d0)
    factor = jnp.block([[d0, zero], [l10, d1]])
    inverse = jnp.block([[g0, zero], [g10, g1]])

    right = dot(inverse, lead_block.reshape(lead, cols_local * block_size))
    left = lax.dot_general(
        jnp.concatenate([row_0, row_1], axis=1), inverse, (((1,), (1,)), ((), ())), precision=HIGHEST
    )
    left = jnp.where(
        row_id == 0,
        factor[:block_size],
        jnp.where(row_id == 1, factor[block_size:], left),
    )
    update = dot(left, right).reshape(block_size, cols_local, block_size)
    trailing = jnp.where(row_id >= PANELS, tiles - update, 0.0)
    panel = jnp.where(col_id == 0, left[:, :block_size], left[:, block_size:])
    first_col = jnp.where(col_id < PANELS, panel, trailing[:, 0, :])
    out = trailing.at[:, 0, :].set(first_col)
    return out.reshape(kernel.shape)


def solution(mesh):
    in_specs = (P(None, "row", None, None, "col", None),)
    out_specs = P(None, "row", None, None, "col", None)
    return jax.shard_map(shards, mesh=mesh, in_specs=in_specs, out_specs=out_specs, check_vma=False)
```

```python
import jax
import jax.numpy as jnp
from jax import lax
from jax.scipy.linalg import solve_triangular
from jax.sharding import PartitionSpec as P

PANELS = 2
HIGHEST = lax.Precision.HIGHEST


def dot(a, b):
    return jnp.dot(a, b, precision=HIGHEST)


def col_rounds(have=PANELS):
    col_devs = lax.axis_size("col")
    rounds = []
    while have < col_devs:
        rounds.append((have, [(i, i + have) for i in range(have) if i + have < col_devs]))
        have *= 2
    return rounds


def tree_round(payload, have, pairs):
    col_id = lax.axis_index("col")
    got = lax.ppermute(payload, "col", pairs)
    return jnp.where((col_id >= have) & (col_id < 2 * have), got, payload)


def from_lead_cols(payload, have=PANELS):
    for have, pairs in col_rounds(have):
        payload = tree_round(payload, have, pairs)
    return payload


def swap_lead_cols(mine):
    col_id = lax.axis_index("col")
    other = lax.ppermute(mine, "col", [(0, 1), (1, 0)])
    return jnp.where(col_id == 0, mine, other), jnp.where(col_id == 0, other, mine)


def blocked_factor(matrix, step):
    count = matrix.shape[0] // step
    blocks = [[matrix[i * step:(i + 1) * step, j * step:(j + 1) * step] for j in range(count)] for i in range(count)]
    eye = jnp.eye(step, dtype=jnp.float32)
    low = [[None] * count for _ in range(count)]
    inv_diag = []
    for k in range(count):
        diag = lax.linalg.cholesky(blocks[k][k], symmetrize_input=False)
        inv = solve_triangular(diag, eye, lower=True)
        low[k][k] = diag
        inv_diag.append(inv)
        if k + 1 < count:
            below = jnp.concatenate([blocks[i][k] for i in range(k + 1, count)], axis=0)
            below = lax.dot_general(below, inv, (((1,), (1,)), ((), ())), precision=HIGHEST)
            for i in range(k + 1, count):
                low[i][k] = below[(i - k - 1) * step:(i - k) * step]
            shrink = lax.dot_general(below, below, (((1,), (1,)), ((), ())), precision=HIGHEST)
            for i in range(k + 1, count):
                for j in range(k + 1, i + 1):
                    blocks[i][j] = blocks[i][j] - shrink[(i - k - 1) * step:(i - k) * step, (j - k - 1) * step:(j - k) * step]
    inverse = [[None] * count for _ in range(count)]
    for j in range(count):
        inverse[j][j] = inv_diag[j]
        for i in range(j + 1, count):
            acc = dot(low[i][j], inverse[j][j])
            for k in range(j + 1, i):
                acc = acc + dot(low[i][k], inverse[k][j])
            inverse[i][j] = -dot(inv_diag[i], acc)
    zero = jnp.zeros((step, step), jnp.float32)
    factor = jnp.block([[low[i][j] if j <= i else zero for j in range(count)] for i in range(count)])
    inverse = jnp.block([[inverse[i][j] if j <= i else zero for j in range(count)] for i in range(count)])
    return factor, inverse


def row_broadcast(blocks, source=0):
    row_devs = lax.axis_size("row")
    shape = blocks.shape
    send = blocks.reshape(row_devs, -1)
    piece = lax.all_to_all(send, "row", 0, 0)[source]
    send = jnp.broadcast_to(piece[None], (row_devs,) + piece.shape)
    return lax.all_to_all(send, "row", 0, 0).reshape(shape)


def lead_rows_from(blocks):
    row_devs = lax.axis_size("row")
    send = blocks.reshape(row_devs, -1)
    piece = lax.all_to_all(send, "row", 0, 0)[:PANELS]
    send = jnp.broadcast_to(piece[None], (row_devs,) + piece.shape)
    gathered = lax.all_to_all(send, "row", 0, 0)
    return gathered.swapaxes(0, 1).reshape((PANELS,) + blocks.shape)


def shards(kernel):
    _, _, block_size, cols_local, _, _ = kernel.shape
    row_devs = lax.axis_size("row")
    row_id = lax.axis_index("row")
    col_id = lax.axis_index("col")
    lead = PANELS * block_size
    piece = block_size // row_devs
    tiles = kernel.reshape(block_size, cols_local, block_size)

    first, second = swap_lead_cols(tiles[:, 0, :])
    held = from_lead_cols(jnp.stack([first, second]))

    send = tiles.reshape(row_devs, piece, cols_local, block_size)
    spread = lax.all_to_all(send, "row", 0, 0)[:PANELS]
    spread, held = lax.optimization_barrier((spread, held))
    row_0, row_1 = held[0], held[1]

    half = block_size // 2
    size = block_size * block_size
    from_row_0 = jnp.concatenate([held[0].ravel(), held[1][:, :half].ravel()])
    from_row_1 = jnp.concatenate([held[1].ravel(), held[0][half:, :].ravel()])
    lead_rows = lead_rows_from(jnp.where(row_id == 0, from_row_0, from_row_1))
    m00 = lead_rows[0, :size].reshape(block_size, block_size)
    m11 = lead_rows[1, :size].reshape(block_size, block_size)
    m10 = jnp.concatenate(
        [lead_rows[0, size:].reshape(block_size, half).T, lead_rows[1, size:].reshape(half, block_size)]
    )
    spread, m00 = lax.optimization_barrier((spread, m00))

    send = jnp.broadcast_to(spread[None], (row_devs,) + spread.shape)
    gathered = lax.all_to_all(send, "row", 0, 0)
    lead_block = gathered.transpose(1, 0, 2, 3, 4).reshape(PANELS, block_size, cols_local, block_size)

    d0, g0 = blocked_factor(m00, 128)
    l10 = lax.dot_general(m10, g0, (((1,), (1,)), ((), ())), precision=HIGHEST)
    schur = m11 - lax.dot_general(l10, l10, (((1,), (1,)), ((), ())), precision=HIGHEST)
    d1, g1 = blocked_factor(schur, 128)
    g10 = -dot(g1, dot(l10, g0))
    zero = jnp.zeros_like(d0)
    factor = jnp.block([[d0, zero], [l10, d1]])
    inverse = jnp.block([[g0, zero], [g10, g1]])

    right = dot(inverse, lead_block.reshape(lead, cols_local * block_size))
    left = lax.dot_general(
        jnp.concatenate([row_0, row_1], axis=1), inverse, (((1,), (1,)), ((), ())), precision=HIGHEST
    )
    left = jnp.where(
        row_id == 0,
        factor[:block_size],
        jnp.where(row_id == 1, factor[block_size:], left),
    )
    update = dot(left, right).reshape(block_size, cols_local, block_size)
    panel = jnp.where(col_id == 0, left[:, :block_size], left[:, block_size:])
    first_local = (jnp.arange(cols_local) == 0)[None, :, None]
    out = jnp.where(
        first_local & (col_id < PANELS),
        panel[:, None, :],
        jnp.where(row_id >= PANELS, tiles - update, 0.0),
    )
    return out.reshape(kernel.shape)


def solution(mesh):
    in_specs = (P(None, "row", None, None, "col", None),)
    out_specs = P(None, "row", None, None, "col", None)
    return jax.shard_map(shards, mesh=mesh, in_specs=in_specs, out_specs=out_specs, check_vma=False)
```

```python
import jax
import jax.numpy as jnp
from jax import lax
from jax.scipy.linalg import solve_triangular
from jax.sharding import PartitionSpec as P

PANELS = 2
HIGHEST = lax.Precision.HIGHEST


def dot(a, b):
    return jnp.dot(a, b, precision=HIGHEST)


def col_rounds(have=PANELS):
    col_devs = lax.axis_size("col")
    rounds = []
    while have < col_devs:
        rounds.append((have, [(i, i + have) for i in range(have) if i + have < col_devs]))
        have *= 2
    return rounds


def tree_round(payload, have, pairs):
    col_id = lax.axis_index("col")
    got = lax.ppermute(payload, "col", pairs)
    return jnp.where((col_id >= have) & (col_id < 2 * have), got, payload)


def from_lead_cols(payload, have=PANELS):
    for have, pairs in col_rounds(have):
        payload = tree_round(payload, have, pairs)
    return payload


def swap_lead_cols(mine):
    col_id = lax.axis_index("col")
    other = lax.ppermute(mine, "col", [(0, 1), (1, 0)])
    return jnp.where(col_id == 0, mine, other), jnp.where(col_id == 0, other, mine)


def blocked_factor(matrix, step):
    count = matrix.shape[0] // step
    blocks = [[matrix[i * step:(i + 1) * step, j * step:(j + 1) * step] for j in range(count)] for i in range(count)]
    eye = jnp.eye(step, dtype=jnp.float32)
    low = [[None] * count for _ in range(count)]
    inv_diag = []
    for k in range(count):
        diag = jnp.linalg.cholesky(blocks[k][k])
        inv = solve_triangular(diag, eye, lower=True)
        low[k][k] = diag
        inv_diag.append(inv)
        if k + 1 < count:
            below = jnp.concatenate([blocks[i][k] for i in range(k + 1, count)], axis=0)
            below = lax.dot_general(below, inv, (((1,), (1,)), ((), ())), precision=HIGHEST)
            for i in range(k + 1, count):
                low[i][k] = below[(i - k - 1) * step:(i - k) * step]
            shrink = lax.dot_general(below, below, (((1,), (1,)), ((), ())), precision=HIGHEST)
            for i in range(k + 1, count):
                for j in range(k + 1, i + 1):
                    blocks[i][j] = blocks[i][j] - shrink[(i - k - 1) * step:(i - k) * step, (j - k - 1) * step:(j - k) * step]
    inverse = [[None] * count for _ in range(count)]
    for j in range(count):
        inverse[j][j] = inv_diag[j]
        for i in range(j + 1, count):
            acc = dot(low[i][j], inverse[j][j])
            for k in range(j + 1, i):
                acc = acc + dot(low[i][k], inverse[k][j])
            inverse[i][j] = -dot(inv_diag[i], acc)
    zero = jnp.zeros((step, step), jnp.float32)
    factor = jnp.block([[low[i][j] if j <= i else zero for j in range(count)] for i in range(count)])
    inverse = jnp.block([[inverse[i][j] if j <= i else zero for j in range(count)] for i in range(count)])
    return factor, inverse


def row_broadcast(blocks, source=0):
    row_devs = lax.axis_size("row")
    shape = blocks.shape
    send = blocks.reshape(row_devs, -1)
    piece = lax.all_to_all(send, "row", 0, 0)[source]
    send = jnp.broadcast_to(piece[None], (row_devs,) + piece.shape)
    return lax.all_to_all(send, "row", 0, 0).reshape(shape)


def lead_rows_from(blocks):
    row_devs = lax.axis_size("row")
    send = blocks.reshape(row_devs, -1)
    piece = lax.all_to_all(send, "row", 0, 0)[:PANELS]
    send = jnp.broadcast_to(piece[None], (row_devs,) + piece.shape)
    gathered = lax.all_to_all(send, "row", 0, 0)
    return gathered.swapaxes(0, 1).reshape((PANELS,) + blocks.shape)


def shards(kernel):
    _, _, block_size, cols_local, _, _ = kernel.shape
    row_devs = lax.axis_size("row")
    row_id = lax.axis_index("row")
    col_id = lax.axis_index("col")
    lead = PANELS * block_size
    piece = block_size // row_devs
    tiles = kernel.reshape(block_size, cols_local, block_size)

    first, second = swap_lead_cols(tiles[:, 0, :])
    held = from_lead_cols(jnp.stack([first, second]))

    send = tiles.reshape(row_devs, piece, cols_local, block_size)
    spread = lax.all_to_all(send, "row", 0, 0)[:PANELS]
    spread, held = lax.optimization_barrier((spread, held))
    row_0, row_1 = held[0], held[1]

    first, second = swap_lead_cols(spread[:, :, 0, :])
    pieces = from_lead_cols(jnp.stack([first[0], first[1], second[1]]))
    send = jnp.broadcast_to(pieces[None], (row_devs,) + pieces.shape)
    lead_rows = lax.all_to_all(send, "row", 0, 0).swapaxes(0, 1).reshape(3, block_size, block_size)
    m00, m10, m11 = lead_rows[0], lead_rows[1], lead_rows[2]
    spread, m00 = lax.optimization_barrier((spread, m00))

    send = jnp.broadcast_to(spread[None], (row_devs,) + spread.shape)
    gathered = lax.all_to_all(send, "row", 0, 0)
    lead_block = gathered.transpose(1, 0, 2, 3, 4).reshape(PANELS, block_size, cols_local, block_size)

    d0, g0 = blocked_factor(m00, 128)
    l10 = lax.dot_general(m10, g0, (((1,), (1,)), ((), ())), precision=HIGHEST)
    schur = m11 - lax.dot_general(l10, l10, (((1,), (1,)), ((), ())), precision=HIGHEST)
    d1, g1 = blocked_factor(schur, 128)
    g10 = -dot(g1, dot(l10, g0))
    zero = jnp.zeros_like(d0)
    factor = jnp.block([[d0, zero], [l10, d1]])
    inverse = jnp.block([[g0, zero], [g10, g1]])

    right = dot(inverse, lead_block.reshape(lead, cols_local * block_size))
    left = lax.dot_general(
        jnp.concatenate([row_0, row_1], axis=1), inverse, (((1,), (1,)), ((), ())), precision=HIGHEST
    )
    left = jnp.where(
        row_id == 0,
        factor[:block_size],
        jnp.where(row_id == 1, factor[block_size:], left),
    )
    update = dot(left, right).reshape(block_size, cols_local, block_size)
    trailing = jnp.where(row_id >= PANELS, tiles - update, 0.0)
    panel = jnp.where(col_id == 0, left[:, :block_size], left[:, block_size:])
    first_col = jnp.where(col_id < PANELS, panel, trailing[:, 0, :])
    out = trailing.at[:, 0, :].set(first_col)
    return out.reshape(kernel.shape)


def solution(mesh):
    in_specs = (P(None, "row", None, None, "col", None),)
    out_specs = P(None, "row", None, None, "col", None)
    return jax.shard_map(shards, mesh=mesh, in_specs=in_specs, out_specs=out_specs, check_vma=False)
```

```python
import jax
import jax.numpy as jnp
from jax import lax
from jax.scipy.linalg import solve_triangular
from jax.sharding import PartitionSpec as P

PANELS = 2
HIGHEST = lax.Precision.HIGHEST


def dot(a, b):
    return jnp.dot(a, b, precision=HIGHEST)


def col_rounds(have=PANELS):
    col_devs = lax.axis_size("col")
    rounds = []
    while have < col_devs:
        rounds.append((have, [(i, i + have) for i in range(have) if i + have < col_devs]))
        have *= 2
    return rounds


def tree_round(payload, have, pairs):
    col_id = lax.axis_index("col")
    got = lax.ppermute(payload, "col", pairs)
    return jnp.where((col_id >= have) & (col_id < 2 * have), got, payload)


def from_lead_cols(payload, have=PANELS):
    for have, pairs in col_rounds(have):
        payload = tree_round(payload, have, pairs)
    return payload


def swap_lead_cols(mine):
    col_id = lax.axis_index("col")
    other = lax.ppermute(mine, "col", [(0, 1), (1, 0)])
    return jnp.where(col_id == 0, mine, other), jnp.where(col_id == 0, other, mine)


def blocked_factor(matrix, step):
    count = matrix.shape[0] // step
    blocks = [[matrix[i * step:(i + 1) * step, j * step:(j + 1) * step] for j in range(count)] for i in range(count)]
    eye = jnp.eye(step, dtype=jnp.float32)
    low = [[None] * count for _ in range(count)]
    inv_diag = []
    for k in range(count):
        diag = jnp.linalg.cholesky(blocks[k][k])
        inv = solve_triangular(diag, eye, lower=True)
        low[k][k] = diag
        inv_diag.append(inv)
        if k + 1 < count:
            below = jnp.concatenate([blocks[i][k] for i in range(k + 1, count)], axis=0)
            below = lax.dot_general(below, inv, (((1,), (1,)), ((), ())), precision=HIGHEST)
            for i in range(k + 1, count):
                low[i][k] = below[(i - k - 1) * step:(i - k) * step]
            shrink = lax.dot_general(below, below, (((1,), (1,)), ((), ())), precision=HIGHEST)
            for i in range(k + 1, count):
                for j in range(k + 1, i + 1):
                    blocks[i][j] = blocks[i][j] - shrink[(i - k - 1) * step:(i - k) * step, (j - k - 1) * step:(j - k) * step]
    inverse = [[None] * count for _ in range(count)]
    for j in range(count):
        inverse[j][j] = inv_diag[j]
        for i in range(j + 1, count):
            acc = dot(low[i][j], inverse[j][j])
            for k in range(j + 1, i):
                acc = acc + dot(low[i][k], inverse[k][j])
            inverse[i][j] = -dot(inv_diag[i], acc)
    zero = jnp.zeros((step, step), jnp.float32)
    factor = jnp.block([[low[i][j] if j <= i else zero for j in range(count)] for i in range(count)])
    inverse = jnp.block([[inverse[i][j] if j <= i else zero for j in range(count)] for i in range(count)])
    return factor, inverse


def row_broadcast(blocks, source=0):
    row_devs = lax.axis_size("row")
    shape = blocks.shape
    send = blocks.reshape(row_devs, -1)
    piece = lax.all_to_all(send, "row", 0, 0)[source]
    send = jnp.broadcast_to(piece[None], (row_devs,) + piece.shape)
    return lax.all_to_all(send, "row", 0, 0).reshape(shape)


def lead_rows_from(blocks):
    row_devs = lax.axis_size("row")
    send = blocks.reshape(row_devs, -1)
    piece = lax.all_to_all(send, "row", 0, 0)[:PANELS]
    send = jnp.broadcast_to(piece[None], (row_devs,) + piece.shape)
    gathered = lax.all_to_all(send, "row", 0, 0)
    return gathered.swapaxes(0, 1).reshape((PANELS,) + blocks.shape)


def shards(kernel):
    _, _, block_size, cols_local, _, _ = kernel.shape
    row_devs = lax.axis_size("row")
    row_id = lax.axis_index("row")
    col_id = lax.axis_index("col")
    lead = PANELS * block_size
    piece = block_size // row_devs
    tiles = kernel.reshape(block_size, cols_local, block_size)

    first, second = swap_lead_cols(tiles[:, 0, :])
    held = from_lead_cols(jnp.stack([first, second]))

    row_0, row_1 = held[0], held[1]

    half = block_size // 2
    size = block_size * block_size
    from_row_0 = jnp.concatenate([held[0].ravel(), held[1][:, :half].ravel()])
    from_row_1 = jnp.concatenate([held[1].ravel(), held[0][half:, :].ravel()])
    lead_rows = lead_rows_from(jnp.where(row_id == 0, from_row_0, from_row_1))
    m00 = lead_rows[0, :size].reshape(block_size, block_size)
    m11 = lead_rows[1, :size].reshape(block_size, block_size)
    m10 = jnp.concatenate(
        [lead_rows[0, size:].reshape(block_size, half).T, lead_rows[1, size:].reshape(half, block_size)]
    )
    tiles_now, m00 = lax.optimization_barrier((tiles, m00))
    send = tiles_now.reshape(row_devs, piece, cols_local, block_size)
    spread = lax.all_to_all(send, "row", 0, 0)[:PANELS]

    send = jnp.broadcast_to(spread[None], (row_devs,) + spread.shape)
    gathered = lax.all_to_all(send, "row", 0, 0)
    lead_block = gathered.transpose(1, 0, 2, 3, 4).reshape(PANELS, block_size, cols_local, block_size)

    d0, g0 = blocked_factor(m00, 128)
    l10 = lax.dot_general(m10, g0, (((1,), (1,)), ((), ())), precision=HIGHEST)
    schur = m11 - lax.dot_general(l10, l10, (((1,), (1,)), ((), ())), precision=HIGHEST)
    d1, g1 = blocked_factor(schur, 128)
    g10 = -dot(g1, dot(l10, g0))
    zero = jnp.zeros_like(d0)
    factor = jnp.block([[d0, zero], [l10, d1]])
    inverse = jnp.block([[g0, zero], [g10, g1]])

    right = dot(inverse, lead_block.reshape(lead, cols_local * block_size))
    left = lax.dot_general(
        jnp.concatenate([row_0, row_1], axis=1), inverse, (((1,), (1,)), ((), ())), precision=HIGHEST
    )
    left = jnp.where(
        row_id == 0,
        factor[:block_size],
        jnp.where(row_id == 1, factor[block_size:], left),
    )
    update = dot(left, right).reshape(block_size, cols_local, block_size)
    trailing = jnp.where(row_id >= PANELS, tiles - update, 0.0)
    panel = jnp.where(col_id == 0, left[:, :block_size], left[:, block_size:])
    first_col = jnp.where(col_id < PANELS, panel, trailing[:, 0, :])
    out = trailing.at[:, 0, :].set(first_col)
    return out.reshape(kernel.shape)


def solution(mesh):
    in_specs = (P(None, "row", None, None, "col", None),)
    out_specs = P(None, "row", None, None, "col", None)
    return jax.shard_map(shards, mesh=mesh, in_specs=in_specs, out_specs=out_specs, check_vma=False)
```

```python
import jax
import jax.numpy as jnp
from jax import lax
from jax.scipy.linalg import solve_triangular
from jax.sharding import PartitionSpec as P

PANELS = 2
HIGHEST = lax.Precision.HIGHEST


def dot(a, b):
    return jnp.dot(a, b, precision=HIGHEST)


def col_rounds(have=PANELS):
    col_devs = lax.axis_size("col")
    rounds = []
    while have < col_devs:
        rounds.append((have, [(i, i + have) for i in range(have) if i + have < col_devs]))
        have *= 2
    return rounds


def tree_round(payload, have, pairs):
    col_id = lax.axis_index("col")
    got = lax.ppermute(payload, "col", pairs)
    return jnp.where((col_id >= have) & (col_id < 2 * have), got, payload)


def from_lead_cols(payload, have=PANELS):
    for have, pairs in col_rounds(have):
        payload = tree_round(payload, have, pairs)
    return payload


def swap_lead_cols(mine):
    col_id = lax.axis_index("col")
    other = lax.ppermute(mine, "col", [(0, 1), (1, 0)])
    return jnp.where(col_id == 0, mine, other), jnp.where(col_id == 0, other, mine)


def blocked_factor(matrix, step):
    count = matrix.shape[0] // step
    blocks = [[matrix[i * step:(i + 1) * step, j * step:(j + 1) * step] for j in range(count)] for i in range(count)]
    eye = jnp.eye(step, dtype=jnp.float32)
    low = [[None] * count for _ in range(count)]
    inv_diag = []
    for k in range(count):
        diag = jnp.linalg.cholesky(blocks[k][k])
        inv = solve_triangular(diag, eye, lower=True)
        low[k][k] = diag
        inv_diag.append(inv)
        if k + 1 < count:
            below = jnp.concatenate([blocks[i][k] for i in range(k + 1, count)], axis=0)
            below = lax.dot_general(below, inv, (((1,), (1,)), ((), ())), precision=HIGHEST)
            for i in range(k + 1, count):
                low[i][k] = below[(i - k - 1) * step:(i - k) * step]
            shrink = lax.dot_general(below, below, (((1,), (1,)), ((), ())), precision=HIGHEST)
            for i in range(k + 1, count):
                for j in range(k + 1, i + 1):
                    blocks[i][j] = blocks[i][j] - shrink[(i - k - 1) * step:(i - k) * step, (j - k - 1) * step:(j - k) * step]
    inverse = [[None] * count for _ in range(count)]
    for j in range(count):
        inverse[j][j] = inv_diag[j]
        for i in range(j + 1, count):
            acc = dot(low[i][j], inverse[j][j])
            for k in range(j + 1, i):
                acc = acc + dot(low[i][k], inverse[k][j])
            inverse[i][j] = -dot(inv_diag[i], acc)
    zero = jnp.zeros((step, step), jnp.float32)
    factor = jnp.block([[low[i][j] if j <= i else zero for j in range(count)] for i in range(count)])
    inverse = jnp.block([[inverse[i][j] if j <= i else zero for j in range(count)] for i in range(count)])
    return factor, inverse


def row_broadcast(blocks, source=0):
    row_devs = lax.axis_size("row")
    shape = blocks.shape
    send = blocks.reshape(row_devs, -1)
    piece = lax.all_to_all(send, "row", 0, 0)[source]
    send = jnp.broadcast_to(piece[None], (row_devs,) + piece.shape)
    return lax.all_to_all(send, "row", 0, 0).reshape(shape)


def lead_rows_from(blocks):
    row_devs = lax.axis_size("row")
    send = blocks.reshape(row_devs, -1)
    piece = lax.all_to_all(send, "row", 0, 0)[:PANELS]
    send = jnp.broadcast_to(piece[None], (row_devs,) + piece.shape)
    gathered = lax.all_to_all(send, "row", 0, 0)
    return gathered.swapaxes(0, 1).reshape((PANELS,) + blocks.shape)


def shards(kernel):
    _, _, block_size, cols_local, _, _ = kernel.shape
    row_devs = lax.axis_size("row")
    row_id = lax.axis_index("row")
    col_id = lax.axis_index("col")
    lead = PANELS * block_size
    piece = block_size // row_devs
    tiles = kernel.reshape(block_size, cols_local, block_size)

    first, second = swap_lead_cols(tiles[:, 0, :])
    held = from_lead_cols(jnp.stack([first, second]))

    send = tiles.reshape(row_devs, piece, cols_local, block_size)
    spread = lax.all_to_all(send, "row", 0, 0)[:PANELS]
    spread, held = lax.optimization_barrier((spread, held))
    row_0, row_1 = held[0], held[1]

    half = block_size // 2
    size = block_size * block_size
    from_row_0 = jnp.concatenate([held[0].ravel(), held[1][:, :half].ravel()])
    from_row_1 = jnp.concatenate([held[1].ravel(), held[0][half:, :].ravel()])
    lead_rows = lead_rows_from(jnp.where(row_id == 0, from_row_0, from_row_1))
    m00 = lead_rows[0, :size].reshape(block_size, block_size)
    m11 = lead_rows[1, :size].reshape(block_size, block_size)
    m10 = jnp.concatenate(
        [lead_rows[0, size:].reshape(block_size, half).T, lead_rows[1, size:].reshape(half, block_size)]
    )
    spread, m00 = lax.optimization_barrier((spread, m00))

    send = jnp.broadcast_to(spread[None], (row_devs,) + spread.shape)
    gathered = lax.all_to_all(send, "row", 0, 0)
    lead_block = gathered.transpose(1, 0, 2, 3, 4).reshape(PANELS, block_size, cols_local, block_size)

    d0, g0 = blocked_factor(m00, 128)
    l10 = lax.dot_general(m10, g0, (((1,), (1,)), ((), ())), precision=HIGHEST)
    schur = m11 - lax.dot_general(l10, l10, (((1,), (1,)), ((), ())), precision=HIGHEST)
    d1, g1 = blocked_factor(schur, 128)
    g10 = -dot(g1, dot(l10, g0))
    zero = jnp.zeros_like(d0)
    factor = jnp.block([[d0, zero], [l10, d1]])

    lead_flat = lead_block.reshape(PANELS, block_size, cols_local * block_size)
    right = jnp.concatenate([dot(g0, lead_flat[0]), dot(g10, lead_flat[0]) + dot(g1, lead_flat[1])])
    nt = (((1,), (1,)), ((), ()))
    left = jnp.concatenate(
        [
            lax.dot_general(row_0, g0, nt, precision=HIGHEST),
            lax.dot_general(row_0, g10, nt, precision=HIGHEST) + lax.dot_general(row_1, g1, nt, precision=HIGHEST),
        ],
        axis=1,
    )
    left = jnp.where(
        row_id == 0,
        factor[:block_size],
        jnp.where(row_id == 1, factor[block_size:], left),
    )
    update = dot(left, right).reshape(block_size, cols_local, block_size)
    trailing = jnp.where(row_id >= PANELS, tiles - update, 0.0)
    panel = jnp.where(col_id == 0, left[:, :block_size], left[:, block_size:])
    first_col = jnp.where(col_id < PANELS, panel, trailing[:, 0, :])
    out = trailing.at[:, 0, :].set(first_col)
    return out.reshape(kernel.shape)


def solution(mesh):
    in_specs = (P(None, "row", None, None, "col", None),)
    out_specs = P(None, "row", None, None, "col", None)
    return jax.shard_map(shards, mesh=mesh, in_specs=in_specs, out_specs=out_specs, check_vma=False)
```
